128 devices in a mesh: pair: 16 (over y_lo, x, core), col: 8 (over y_hi, z).
Axes of the slice: x: 4, y: 4 (y_hi: 2, y_lo: 2; y = y_hi * 2 + y_lo), z: 4, core: 2. Of those that a mesh axis runs over, the one named last changes fastest.
Arguments:
- tmatrix: bfloat16 [16, 2, 4096, 4096], P('pair', None, None, 'col'), may hold values from -0.046875 to 0.046875
- translation: bfloat16 [16, 2, 4096, 4096], P('pair', None, None, 'col'), may hold values from -0.0625 to 0.0625
- incident: bfloat16 [16, 4096, 256], P('pair', 'col'), may hold values from -6 to 6
- farfield: bfloat16 [2, 2048, 4096], P(None, None, 'col'), may hold values from -0.0625 to 0.0625
- centres: int32 [16, 3], replicated, may hold values from -8 to 8
Outputs:
- amplitude: float32 [16, 2048, 128], P('pair', 'col')
The draws below stay inside these ranges and needn't reach their ends.
All inputs are finite; a program needn't handle non-finite values.
Results may differ from the reference program's by a relative error of at most 0.034.
Values may be sent and summed in bfloat16 or wider, within the bound.
No kernel may reach another device: no remote copies, remote signals or barrier semaphores. Data moves between devices by JAX's collectives and lax.ppermute only.
A program may use at most 128 MiB of HBM per device.

```python
import math
import jax
import jax.numpy as jnp
from jax import lax

M = 4096
K = 128
S = 2048
ITERS = 3
LEVEL = 2
MC = 512
KH = 64
CLUSTERS = 16
N_COL = 8


def set_ends(entries, stream_key, least, high):
    dims = entries.shape
    spot = [jax.random.randint(jax.random.fold_in(stream_key, axis), (), 0, dims[axis]) for axis in range(len(dims))]
    entries = entries.at[tuple(spot)].set(least)
    longest = dims.index(max(dims))
    spot[longest] = (spot[longest] + 1) % dims[longest]
    return entries.at[tuple(spot)].set(high)


def level_of(own_key, dims, cuts, low, high):
    level = 1.0
    for position, parts in cuts:
        steps = jax.random.uniform(jax.random.fold_in(jax.random.fold_in(own_key, 6), position), (parts,), jnp.float32, low / len(cuts), high / len(cuts))
        level = level * jnp.repeat(jnp.exp(steps), dims[position] // parts).reshape((-1,) + (1,) * (len(dims) - 1 - position))
    return level


def normal_values(own_key, shape, width, bound, cuts=(), held_as=jnp.bfloat16):
    entries = jax.random.normal(own_key, shape, jnp.float32) * width
    if len(cuts) > 0:
        entries = level_of(own_key, shape, cuts, -0.22, 0.18) * entries
    return jnp.clip(entries, min=-bound, max=bound).astype(held_as)


def setup_inputs(seed: int = 0) -> dict:
    streams_of = jax.random.split(jax.random.key(seed), 6)
    return {
        "tmatrix": normal_values(streams_of[0], (CLUSTERS, 2, M, M), (4 * M) ** -0.5, 0.046875, ((0, 16), (3, 8))),
        "translation": normal_values(streams_of[1], (CLUSTERS, 2, M, M), (2 * M) ** -0.5, 0.0625, ((0, 16), (3, 8))),
        "incident": normal_values(streams_of[2], (CLUSTERS, M, 2 * K), 1.0, 6.0, ((0, 16), (1, 8))),
        "farfield": normal_values(streams_of[3], (2, S, M), (2 * M) ** -0.5, 0.0625, ((2, 8),)),
        "centres": set_ends(jax.random.randint(streams_of[4], (CLUSTERS, 3), -8, 9), jax.random.fold_in(streams_of[4], 1), -8, 8).astype(jnp.int32),
    }


def turned_block(vector):
    half_width = vector.shape[1] // 2
    return jnp.concatenate([-vector[:, half_width:], vector[:, :half_width]], axis=1)


def panel_sum(matrix, vector):
    turned = turned_block(vector)
    total = jnp.zeros((matrix.shape[1], vector.shape[1]), jnp.float32)
    for block_index in range(N_COL):
        offset = block_index * MC
        partial_term = jnp.dot(matrix[0][:, offset:offset + MC], vector[offset:offset + MC], preferred_element_type=jnp.float32)
        partial_term = partial_term + jnp.dot(matrix[1][:, offset:offset + MC], turned[offset:offset + MC], preferred_element_type=jnp.float32)
        rounded = lax.optimization_barrier(partial_term.astype(jnp.bfloat16))
        total = total + rounded.astype(jnp.float32)
    return total


def direction_phase(centre):
    steps_int = jnp.arange(S, dtype=jnp.int32)
    polar = (math.pi / S) * (steps_int.astype(jnp.float32) + 0.5)
    azimuth = (2.0 * math.pi / 97.0) * ((steps_int * 40) % 97).astype(jnp.float32)
    spot = centre.astype(jnp.float32)
    return 0.7 * (jnp.sin(polar) * jnp.cos(azimuth) * spot[0] + jnp.sin(polar) * jnp.sin(azimuth) * spot[1] + jnp.cos(polar) * spot[2])


def rotate(field, phase):
    half_width = field.shape[1] // 2
    cosine = jnp.cos(phase)[:, None]
    sine = jnp.sin(phase)[:, None]
    real_part = field[:, :half_width]
    imag_part = field[:, half_width:]
    return jnp.concatenate([cosine * real_part + sine * imag_part, cosine * imag_part - sine * real_part], axis=1)


def far_field(farfield, coeffs):
    return jnp.dot(farfield[0], coeffs, preferred_element_type=jnp.float32) + jnp.dot(farfield[1], turned_block(coeffs), preferred_element_type=jnp.float32)


def reference(tmatrix, translation, incident, farfield, centres):
    coeffs = [panel_sum(tmatrix[member], incident[member]).astype(jnp.bfloat16) for member in range(CLUSTERS)]
    for iteration in range(ITERS):
        fresh = []
        for member in range(CLUSTERS):
            other = member ^ (1 << LEVEL)
            driven = (incident[member].astype(jnp.float32) + panel_sum(translation[member], coeffs[other])).astype(jnp.bfloat16)
            fresh.append(panel_sum(tmatrix[member], driven).astype(jnp.bfloat16))
        coeffs = fresh
    rotated = [rotate(far_field(farfield, coeffs[member]), direction_phase(centres[member])) for member in range(CLUSTERS)]
    outputs = []
    for member in range(CLUSTERS):
        merged = rotated[member] + rotated[member ^ (1 << LEVEL)]
        column_half = (member >> LEVEL) & 1
        outputs.append(jnp.concatenate([merged[:, column_half * KH:(column_half + 1) * KH], merged[:, K + column_half * KH:K + (column_half + 1) * KH]], axis=1))
    return jnp.stack(outputs)
```

```python
import math

import jax
import jax.numpy as jnp
from jax import lax
from jax.sharding import PartitionSpec as P

ITERS = 3
LEVEL = 2


def partner(value, axis, bit):
    mask = 2**bit
    pairs = [(source, source ^ mask) for source in range(lax.axis_size(axis))]
    return lax.ppermute(value, axis, pairs)


def turned_block(vector):
    half_width = vector.shape[1] // 2
    return jnp.concatenate([-vector[:, half_width:], vector[:, :half_width]], axis=1)


def rotate(field, phase):
    half_width = field.shape[1] // 2
    cosine = jnp.cos(phase)[:, None]
    sine = jnp.sin(phase)[:, None]
    real_part = field[:, :half_width]
    imag_part = field[:, half_width:]
    return jnp.concatenate(
        [cosine * real_part + sine * imag_part, cosine * imag_part - sine * real_part], axis=1
    )


def direction_phase(centre, count, total_rows):
    steps_int = jnp.arange(count, dtype=jnp.int32)
    polar = math.pi / total_rows * (steps_int.astype(jnp.float32) + 0.5)
    azimuth = 2.0 * math.pi / 97.0 * (steps_int * 40 % 97).astype(jnp.float32)
    spot = centre.astype(jnp.float32)
    return 0.7 * (
        jnp.sin(polar) * jnp.cos(azimuth) * spot[0]
        + jnp.sin(polar) * jnp.sin(azimuth) * spot[1]
        + jnp.cos(polar) * spot[2]
    )


def pick_half(vector, column_half, half_width):
    full_width = vector.shape[1] // 2
    real_part = lax.dynamic_slice_in_dim(vector, column_half * half_width, half_width, 1)
    imag_part = lax.dynamic_slice_in_dim(
        vector, full_width + column_half * half_width, half_width, 1
    )
    return jnp.concatenate([real_part, imag_part], axis=1)


def col_sum(partial):
    count = lax.axis_size("col")
    rows, width = partial.shape
    blocks = partial.astype(jnp.bfloat16).reshape(count, rows // count, width)
    received = lax.all_to_all(blocks, "col", 0, 0)
    return jnp.sum(received.astype(jnp.float32), axis=0)


def product(matrix, vector):
    return jnp.dot(matrix[0], vector, preferred_element_type=jnp.float32) + jnp.dot(
        matrix[1], turned_block(vector), preferred_element_type=jnp.float32
    )


def on_device(tmatrix, translation, incident, farfield, centres):
    pair_index = lax.axis_index("pair")
    column_half = jnp.bitwise_and(jnp.right_shift(pair_index, LEVEL), 1)
    own_centre = lax.dynamic_index_in_dim(centres, pair_index, 0, keepdims=False)
    other_centre = lax.dynamic_index_in_dim(
        centres, jnp.bitwise_xor(pair_index, 2**LEVEL), 0, keepdims=False
    )
    own_matrix = tmatrix[0]
    own_coupling = translation[0]
    own_incident = incident[0]
    full_width = own_incident.shape[1] // 2
    half_width = full_width // 2
    coeffs = col_sum(product(own_matrix, own_incident)).astype(jnp.bfloat16)
    for iteration in range(ITERS):
        partner_coeffs = partner(coeffs, "pair", LEVEL)
        driven = (
            own_incident.astype(jnp.float32) + col_sum(product(own_coupling, partner_coeffs))
        ).astype(jnp.bfloat16)
        coeffs = col_sum(product(own_matrix, driven)).astype(jnp.bfloat16)
    incoming = partner(pick_half(coeffs, 1 - column_half, half_width), "pair", LEVEL)
    own_half = pick_half(coeffs, column_half, half_width)
    total_rows = farfield.shape[1]
    both = jnp.concatenate([own_half, incoming], axis=1)
    both_turned = jnp.concatenate([turned_block(own_half), turned_block(incoming)], axis=1)
    field = jnp.dot(farfield[0], both, preferred_element_type=jnp.float32) + jnp.dot(
        farfield[1], both_turned, preferred_element_type=jnp.float32
    )
    width = own_half.shape[1]
    merged = rotate(field[:, :width], direction_phase(own_centre, total_rows, total_rows)) + rotate(
        field[:, width:], direction_phase(other_centre, total_rows, total_rows)
    )
    amplitude = col_sum(merged)
    return amplitude[None]


def solution(mesh):
    return jax.shard_map(
        on_device,
        mesh=mesh,
        in_specs=(
            P("pair", None, None, "col"),
            P("pair", None, None, "col"),
            P("pair", "col", None),
            P(None, None, "col"),
            P(),
        ),
        out_specs=P("pair", "col", None),
        check_vma=False,
    )
```

```python
import math

import jax
import jax.numpy as jnp
from jax import lax
from jax.sharding import PartitionSpec as P

ITERS = 3
LEVEL = 2


def partner(value, axis, bit):
    mask = 2**bit
    pairs = [(source, source ^ mask) for source in range(lax.axis_size(axis))]
    return lax.ppermute(value, axis, pairs)


def turned_block(vector):
    half_width = vector.shape[1] // 2
    return jnp.concatenate([-vector[:, half_width:], vector[:, :half_width]], axis=1)


def rotate(field, phase):
    half_width = field.shape[1] // 2
    cosine = jnp.cos(phase)[:, None]
    sine = jnp.sin(phase)[:, None]
    real_part = field[:, :half_width]
    imag_part = field[:, half_width:]
    return jnp.concatenate(
        [cosine * real_part + sine * imag_part, cosine * imag_part - sine * real_part], axis=1
    )


def direction_phase(centre, count, total_rows):
    steps_int = jnp.arange(count, dtype=jnp.int32)
    polar = math.pi / total_rows * (steps_int.astype(jnp.float32) + 0.5)
    azimuth = 2.0 * math.pi / 97.0 * (steps_int * 40 % 97).astype(jnp.float32)
    spot = centre.astype(jnp.float32)
    return 0.7 * (
        jnp.sin(polar) * jnp.cos(azimuth) * spot[0]
        + jnp.sin(polar) * jnp.sin(azimuth) * spot[1]
        + jnp.cos(polar) * spot[2]
    )


def pick_half(vector, column_half, half_width):
    full_width = vector.shape[1] // 2
    real_part = lax.dynamic_slice_in_dim(vector, column_half * half_width, half_width, 1)
    imag_part = lax.dynamic_slice_in_dim(
        vector, full_width + column_half * half_width, half_width, 1
    )
    return jnp.concatenate([real_part, imag_part], axis=1)


def col_sum(partial):
    count = lax.axis_size("col")
    rows, width = partial.shape
    blocks = partial.astype(jnp.bfloat16).reshape(count, rows // count, width)
    received = lax.all_to_all(blocks, "col", 0, 0)
    return jnp.sum(received.astype(jnp.float32), axis=0)


def product(matrix, vector):
    return jnp.dot(matrix[0], vector, preferred_element_type=jnp.float32) + jnp.dot(
        matrix[1], turned_block(vector), preferred_element_type=jnp.float32
    )


CHUNKS = 2


def column_chunk(vector, index, count):
    full_width = vector.shape[1] // 2
    width = full_width // count
    return jnp.concatenate(
        [
            vector[:, index * width : (index + 1) * width],
            vector[:, full_width + index * width : full_width + (index + 1) * width],
        ],
        axis=1,
    )


def on_device(tmatrix, translation, incident, farfield, centres):
    pair_index = lax.axis_index("pair")
    column_half = jnp.bitwise_and(jnp.right_shift(pair_index, LEVEL), 1)
    own_centre = lax.dynamic_index_in_dim(centres, pair_index, 0, keepdims=False)
    other_centre = lax.dynamic_index_in_dim(
        centres, jnp.bitwise_xor(pair_index, 2**LEVEL), 0, keepdims=False
    )
    own_matrix = tmatrix[0]
    own_coupling = translation[0]
    own_incident = incident[0]
    chunk_incident = [column_chunk(own_incident, j, CHUNKS) for j in range(CHUNKS)]
    coeffs = [
        col_sum(product(own_matrix, chunk_incident[j])).astype(jnp.bfloat16) for j in range(CHUNKS)
    ]
    for iteration in range(ITERS):
        fresh = []
        for j in range(CHUNKS):
            partner_coeffs = partner(coeffs[j], "pair", LEVEL)
            driven = (
                chunk_incident[j].astype(jnp.float32)
                + col_sum(product(own_coupling, partner_coeffs))
            ).astype(jnp.bfloat16)
            fresh.append(col_sum(product(own_matrix, driven)).astype(jnp.bfloat16))
        coeffs = fresh
    received = [partner(coeffs[j], "pair", LEVEL) for j in range(CHUNKS)]
    per_half = CHUNKS // 2

    def half_of(parts):
        width = parts[0].shape[1] // 2
        pieces = [jnp.where(column_half == 0, parts[i], parts[per_half + i]) for i in range(per_half)]
        real_part = jnp.concatenate([piece[:, :width] for piece in pieces], axis=1)
        imag_part = jnp.concatenate([piece[:, width:] for piece in pieces], axis=1)
        return jnp.concatenate([real_part, imag_part], axis=1)

    own_half = half_of(coeffs)
    incoming = half_of(received)
    total_rows = farfield.shape[1]
    both = jnp.concatenate([own_half, incoming], axis=1)
    both_turned = jnp.concatenate([turned_block(own_half), turned_block(incoming)], axis=1)
    field = jnp.dot(farfield[0], both, preferred_element_type=jnp.float32) + jnp.dot(
        farfield[1], both_turned, preferred_element_type=jnp.float32
    )
    width = own_half.shape[1]
    merged = rotate(field[:, :width], direction_phase(own_centre, total_rows, total_rows)) + rotate(
        field[:, width:], direction_phase(other_centre, total_rows, total_rows)
    )
    amplitude = col_sum(merged)
    return amplitude[None]


def solution(mesh):
    return jax.shard_map(
        on_device,
        mesh=mesh,
        in_specs=(
            P("pair", None, None, "col"),
            P("pair", None, None, "col"),
            P("pair", "col", None),
            P(None, None, "col"),
            P(),
        ),
        out_specs=P("pair", "col", None),
        check_vma=False,
    )
```

```python
import math

import jax
import jax.numpy as jnp
from jax import lax
from jax.sharding import PartitionSpec as P

ITERS = 3
LEVEL = 2


def partner(value, axis, bit):
    mask = 2**bit
    pairs = [(source, source ^ mask) for source in range(lax.axis_size(axis))]
    return lax.ppermute(value, axis, pairs)


def turned_block(vector):
    half_width = vector.shape[1] // 2
    return jnp.concatenate([-vector[:, half_width:], vector[:, :half_width]], axis=1)


def rotate(field, phase):
    half_width = field.shape[1] // 2
    cosine = jnp.cos(phase)[:, None]
    sine = jnp.sin(phase)[:, None]
    real_part = field[:, :half_width]
    imag_part = field[:, half_width:]
    return jnp.concatenate(
        [cosine * real_part + sine * imag_part, cosine * imag_part - sine * real_part], axis=1
    )


def direction_phase(centre, count, total_rows):
    steps_int = jnp.arange(count, dtype=jnp.int32)
    polar = math.pi / total_rows * (steps_int.astype(jnp.float32) + 0.5)
    azimuth = 2.0 * math.pi / 97.0 * (steps_int * 40 % 97).astype(jnp.float32)
    spot = centre.astype(jnp.float32)
    return 0.7 * (
        jnp.sin(polar) * jnp.cos(azimuth) * spot[0]
        + jnp.sin(polar) * jnp.sin(azimuth) * spot[1]
        + jnp.cos(polar) * spot[2]
    )


def pick_half(vector, column_half, half_width):
    full_width = vector.shape[1] // 2
    real_part = lax.dynamic_slice_in_dim(vector, column_half * half_width, half_width, 1)
    imag_part = lax.dynamic_slice_in_dim(
        vector, full_width + column_half * half_width, half_width, 1
    )
    return jnp.concatenate([real_part, imag_part], axis=1)


def col_sum(partial):
    count = lax.axis_size("col")
    rows, width = partial.shape
    blocks = partial.astype(jnp.bfloat16).reshape(count, rows // count, width)
    received = lax.all_to_all(blocks, "col", 0, 0)
    return jnp.sum(received.astype(jnp.float32), axis=0)


def partner_sum(partial):
    count = lax.axis_size("col")
    pairs = lax.axis_size("pair")
    rows, width = partial.shape
    blocks = partial.astype(jnp.bfloat16).reshape(count, rows // count, width)
    col_index = lax.axis_index("col")
    total = None
    for offset in range(count):
        send = lax.dynamic_index_in_dim(blocks, (col_index + offset) % count, 0, keepdims=False)
        moves = [
            (source * count + col, (source ^ 2**LEVEL) * count + (col + offset) % count)
            for source in range(pairs)
            for col in range(count)
        ]
        got = lax.ppermute(send, ("pair", "col"), moves).astype(jnp.float32)
        total = got if total is None else total + got
    return total


def product(matrix, vector):
    return jnp.dot(matrix[0], vector, preferred_element_type=jnp.float32) + jnp.dot(
        matrix[1], turned_block(vector), preferred_element_type=jnp.float32
    )


def on_device(tmatrix, translation, incident, farfield, centres):
    pair_index = lax.axis_index("pair")
    column_half = jnp.bitwise_and(jnp.right_shift(pair_index, LEVEL), 1)
    own_centre = lax.dynamic_index_in_dim(centres, pair_index, 0, keepdims=False)
    other_centre = lax.dynamic_index_in_dim(
        centres, jnp.bitwise_xor(pair_index, 2**LEVEL), 0, keepdims=False
    )
    own_matrix = tmatrix[0]
    own_coupling = translation[0]
    own_incident = incident[0]
    full_width = own_incident.shape[1] // 2
    half_width = full_width // 2
    partner_coeffs = partner_sum(product(own_matrix, own_incident)).astype(jnp.bfloat16)
    for iteration in range(ITERS):
        driven = (
            own_incident.astype(jnp.float32) + col_sum(product(own_coupling, partner_coeffs))
        ).astype(jnp.bfloat16)
        if iteration + 1 < ITERS:
            partner_coeffs = partner_sum(product(own_matrix, driven)).astype(jnp.bfloat16)
        else:
            coeffs = col_sum(product(own_matrix, driven)).astype(jnp.bfloat16)
    incoming = partner(pick_half(coeffs, 1 - column_half, half_width), "pair", LEVEL)
    own_half = pick_half(coeffs, column_half, half_width)
    total_rows = farfield.shape[1]
    both = jnp.concatenate([own_half, incoming], axis=1)
    both_turned = jnp.concatenate([turned_block(own_half), turned_block(incoming)], axis=1)
    field = jnp.dot(farfield[0], both, preferred_element_type=jnp.float32) + jnp.dot(
        farfield[1], both_turned, preferred_element_type=jnp.float32
    )
    width = own_half.shape[1]
    merged = rotate(field[:, :width], direction_phase(own_centre, total_rows, total_rows)) + rotate(
        field[:, width:], direction_phase(other_centre, total_rows, total_rows)
    )
    amplitude = col_sum(merged)
    return amplitude[None]


def solution(mesh):
    return jax.shard_map(
        on_device,
        mesh=mesh,
        in_specs=(
            P("pair", None, None, "col"),
            P("pair", None, None, "col"),
            P("pair", "col", None),
            P(None, None, "col"),
            P(),
        ),
        out_specs=P("pair", "col", None),
        check_vma=False,
    )
```

```python
import math

import jax
import jax.numpy as jnp
from jax import lax
from jax.experimental import pallas as pl
from jax.sharding import PartitionSpec as P

ITERS = 3
LEVEL = 2


def partner(value, axis, bit):
    mask = 2**bit
    pairs = [(source, source ^ mask) for source in range(lax.axis_size(axis))]
    return lax.ppermute(value, axis, pairs)


def turned_block(vector):
    half_width = vector.shape[1] // 2
    return jnp.concatenate([-vector[:, half_width:], vector[:, :half_width]], axis=1)


def rotate(field, phase):
    half_width = field.shape[1] // 2
    cosine = jnp.cos(phase)[:, None]
    sine = jnp.sin(phase)[:, None]
    real_part = field[:, :half_width]
    imag_part = field[:, half_width:]
    return jnp.concatenate(
        [cosine * real_part + sine * imag_part, cosine * imag_part - sine * real_part], axis=1
    )


def direction_phase(centre, count, total_rows):
    steps_int = jnp.arange(count, dtype=jnp.int32)
    polar = math.pi / total_rows * (steps_int.astype(jnp.float32) + 0.5)
    azimuth = 2.0 * math.pi / 97.0 * (steps_int * 40 % 97).astype(jnp.float32)
    spot = centre.astype(jnp.float32)
    return 0.7 * (
        jnp.sin(polar) * jnp.cos(azimuth) * spot[0]
        + jnp.sin(polar) * jnp.sin(azimuth) * spot[1]
        + jnp.cos(polar) * spot[2]
    )


def pick_half(vector, column_half, half_width):
    full_width = vector.shape[1] // 2
    real_part = lax.dynamic_slice_in_dim(vector, column_half * half_width, half_width, 1)
    imag_part = lax.dynamic_slice_in_dim(
        vector, full_width + column_half * half_width, half_width, 1
    )
    return jnp.concatenate([real_part, imag_part], axis=1)


def col_sum(partial):
    count = lax.axis_size("col")
    rows, width = partial.shape
    blocks = partial.astype(jnp.bfloat16).reshape(count, rows // count, width)
    received = lax.all_to_all(blocks, "col", 0, 0)
    return jnp.sum(received.astype(jnp.float32), axis=0)


def product_body(matrix_ref, vector_ref, turned_ref, out_ref):
    total = jnp.dot(matrix_ref[0, 0], vector_ref[...], preferred_element_type=jnp.float32)
    total = total + jnp.dot(matrix_ref[0, 1], turned_ref[...], preferred_element_type=jnp.float32)
    out_ref[...] = total.astype(out_ref.dtype)


def product(matrices, vector, block_rows=1024):
    _, _, rows, cols = matrices.shape
    width = vector.shape[1]
    return pl.pallas_call(
        product_body,
        grid=(rows // block_rows,),
        in_specs=[
            pl.BlockSpec((1, 2, block_rows, cols), lambda i: (0, 0, i, 0)),
            pl.BlockSpec((cols, width), lambda i: (0, 0)),
            pl.BlockSpec((cols, width), lambda i: (0, 0)),
        ],
        out_specs=pl.BlockSpec((block_rows, width), lambda i: (i, 0)),
        out_shape=jax.ShapeDtypeStruct((rows, width), jnp.bfloat16),
        cost_estimate=pl.CostEstimate(
            flops=4 * rows * cols * width,
            transcendentals=0,
            bytes_accessed=2 * (2 * rows * cols + 2 * cols * width + rows * width),
        ),
    )(matrices, vector, turned_block(vector))


def on_device(tmatrix, translation, incident, farfield, centres):
    pair_index = lax.axis_index("pair")
    column_half = jnp.bitwise_and(jnp.right_shift(pair_index, LEVEL), 1)
    own_centre = lax.dynamic_index_in_dim(centres, pair_index, 0, keepdims=False)
    other_centre = lax.dynamic_index_in_dim(
        centres, jnp.bitwise_xor(pair_index, 2**LEVEL), 0, keepdims=False
    )
    own_matrix = tmatrix
    own_coupling = translation
    own_incident = incident[0]
    full_width = own_incident.shape[1] // 2
    half_width = full_width // 2
    coeffs = col_sum(product(own_matrix, own_incident)).astype(jnp.bfloat16)
    for iteration in range(ITERS):
        partner_coeffs = partner(coeffs, "pair", LEVEL)
        driven = (
            own_incident.astype(jnp.float32) + col_sum(product(own_coupling, partner_coeffs))
        ).astype(jnp.bfloat16)
        coeffs = col_sum(product(own_matrix, driven)).astype(jnp.bfloat16)
    incoming = partner(pick_half(coeffs, 1 - column_half, half_width), "pair", LEVEL)
    own_half = pick_half(coeffs, column_half, half_width)
    total_rows = farfield.shape[1]
    both = jnp.concatenate([own_half, incoming], axis=1)
    both_turned = jnp.concatenate([turned_block(own_half), turned_block(incoming)], axis=1)
    field = jnp.dot(farfield[0], both, preferred_element_type=jnp.float32) + jnp.dot(
        farfield[1], both_turned, preferred_element_type=jnp.float32
    )
    width = own_half.shape[1]
    merged = rotate(field[:, :width], direction_phase(own_centre, total_rows, total_rows)) + rotate(
        field[:, width:], direction_phase(other_centre, total_rows, total_rows)
    )
    amplitude = col_sum(merged)
    return amplitude[None]


def solution(mesh):
    return jax.shard_map(
        on_device,
        mesh=mesh,
        in_specs=(
            P("pair", None, None, "col"),
            P("pair", None, None, "col"),
            P("pair", "col", None),
            P(None, None, "col"),
            P(),
        ),
        out_specs=P("pair", "col", None),
        check_vma=False,
    )
```

```python
import math

import jax
import jax.numpy as jnp
from jax import lax
from jax.sharding import PartitionSpec as P

ITERS = 3
LEVEL = 2


def partner(value, axis, bit):
    mask = 2**bit
    pairs = [(source, source ^ mask) for source in range(lax.axis_size(axis))]
    return lax.ppermute(value, axis, pairs)


def turned_block(vector):
    half_width = vector.shape[1] // 2
    return jnp.concatenate([-vector[:, half_width:], vector[:, :half_width]], axis=1)


def rotate(field, phase):
    half_width = field.shape[1] // 2
    cosine = jnp.cos(phase)[:, None]
    sine = jnp.sin(phase)[:, None]
    real_part = field[:, :half_width]
    imag_part = field[:, half_width:]
    return jnp.concatenate(
        [cosine * real_part + sine * imag_part, cosine * imag_part - sine * real_part], axis=1
    )


def direction_phase(centre, count, total_rows):
    steps_int = jnp.arange(count, dtype=jnp.int32)
    polar = math.pi / total_rows * (steps_int.astype(jnp.float32) + 0.5)
    azimuth = 2.0 * math.pi / 97.0 * (steps_int * 40 % 97).astype(jnp.float32)
    spot = centre.astype(jnp.float32)
    return 0.7 * (
        jnp.sin(polar) * jnp.cos(azimuth) * spot[0]
        + jnp.sin(polar) * jnp.sin(azimuth) * spot[1]
        + jnp.cos(polar) * spot[2]
    )


def pick_half(vector, column_half, half_width):
    full_width = vector.shape[1] // 2
    real_part = lax.dynamic_slice_in_dim(vector, column_half * half_width, half_width, 1)
    imag_part = lax.dynamic_slice_in_dim(
        vector, full_width + column_half * half_width, half_width, 1
    )
    return jnp.concatenate([real_part, imag_part], axis=1)


def col_sum(partial):
    count = lax.axis_size("col")
    rows, width = partial.shape
    blocks = partial.astype(jnp.bfloat16).reshape(count, rows // count, width)
    received = lax.all_to_all(blocks, "col", 0, 0)
    return jnp.sum(received.astype(jnp.float32), axis=0)


def product(matrix, vector):
    stacked = jnp.stack([vector, turned_block(vector)])
    return jnp.einsum("prc,pck->rk", matrix, stacked, preferred_element_type=jnp.float32)


def on_device(tmatrix, translation, incident, farfield, centres):
    pair_index = lax.axis_index("pair")
    column_half = jnp.bitwise_and(jnp.right_shift(pair_index, LEVEL), 1)
    own_centre = lax.dynamic_index_in_dim(centres, pair_index, 0, keepdims=False)
    other_centre = lax.dynamic_index_in_dim(
        centres, jnp.bitwise_xor(pair_index, 2**LEVEL), 0, keepdims=False
    )
    own_matrix = tmatrix[0]
    own_coupling = translation[0]
    own_incident = incident[0]
    full_width = own_incident.shape[1] // 2
    half_width = full_width // 2
    coeffs = col_sum(product(own_matrix, own_incident)).astype(jnp.bfloat16)
    for iteration in range(ITERS):
        partner_coeffs = partner(coeffs, "pair", LEVEL)
        driven = (
            own_incident.astype(jnp.float32) + col_sum(product(own_coupling, partner_coeffs))
        ).astype(jnp.bfloat16)
        coeffs = col_sum(product(own_matrix, driven)).astype(jnp.bfloat16)
    incoming = partner(pick_half(coeffs, 1 - column_half, half_width), "pair", LEVEL)
    own_half = pick_half(coeffs, column_half, half_width)
    total_rows = farfield.shape[1]
    both = jnp.concatenate([own_half, incoming], axis=1)
    both_turned = jnp.concatenate([turned_block(own_half), turned_block(incoming)], axis=1)
    field = jnp.dot(farfield[0], both, preferred_element_type=jnp.float32) + jnp.dot(
        farfield[1], both_turned, preferred_element_type=jnp.float32
    )
    width = own_half.shape[1]
    merged = rotate(field[:, :width], direction_phase(own_centre, total_rows, total_rows)) + rotate(
        field[:, width:], direction_phase(other_centre, total_rows, total_rows)
    )
    amplitude = col_sum(merged)
    return amplitude[None]


def solution(mesh):
    return jax.shard_map(
        on_device,
        mesh=mesh,
        in_specs=(
            P("pair", None, None, "col"),
            P("pair", None, None, "col"),
            P("pair", "col", None),
            P(None, None, "col"),
            P(),
        ),
        out_specs=P("pair", "col", None),
        check_vma=False,
    )
```

```python
import math

import jax
import jax.numpy as jnp
from jax import lax
from jax.sharding import PartitionSpec as P


ITERS = 3
LEVEL = 2


def partner(value, axis, bit):
    mask = 2**bit
    pairs = [(source, source ^ mask) for source in range(lax.axis_size(axis))]
    return lax.ppermute(value, axis, pairs)


def turned_block(vector):
    half_width = vector.shape[1] // 2
    return jnp.concatenate([-vector[:, half_width:], vector[:, :half_width]], axis=1)


def rotate(field, phase):
    half_width = field.shape[1] // 2
    cosine = jnp.cos(phase)[:, None]
    sine = jnp.sin(phase)[:, None]
    real_part = field[:, :half_width]
    imag_part = field[:, half_width:]
    return jnp.concatenate(
        [cosine * real_part + sine * imag_part, cosine * imag_part - sine * real_part], axis=1
    )


def direction_phase(centre, count, total_rows):
    steps_int = jnp.arange(count, dtype=jnp.int32)
    polar = math.pi / total_rows * (steps_int.astype(jnp.float32) + 0.5)
    azimuth = 2.0 * math.pi / 97.0 * (steps_int * 40 % 97).astype(jnp.float32)
    spot = centre.astype(jnp.float32)
    return 0.7 * (
        jnp.sin(polar) * jnp.cos(azimuth) * spot[0]
        + jnp.sin(polar) * jnp.sin(azimuth) * spot[1]
        + jnp.cos(polar) * spot[2]
    )


def pick_half(vector, column_half, half_width):
    full_width = vector.shape[1] // 2
    real_part = lax.dynamic_slice_in_dim(vector, column_half * half_width, half_width, 1)
    imag_part = lax.dynamic_slice_in_dim(
        vector, full_width + column_half * half_width, half_width, 1
    )
    return jnp.concatenate([real_part, imag_part], axis=1)


def col_sum(partial):
    count = lax.axis_size("col")
    rows, width = partial.shape
    blocks = partial.astype(jnp.bfloat16).reshape(count, rows // count, width)
    received = lax.all_to_all(blocks, "col", 0, 0)
    return jnp.sum(received.astype(jnp.float32), axis=0)


def product(matrix, vector):
    stacked = jnp.stack([vector, turned_block(vector)])
    return jnp.einsum("prc,pck->rk", matrix, stacked, preferred_element_type=jnp.float32)


def split_product(matrix, parts):
    total = None
    start = 0
    for index, piece in enumerate(parts):
        rows = piece.shape[0]
        term = product(matrix[:, :, start : start + rows], piece)
        if index + 1 < len(parts):
            term = lax.optimization_barrier(term)
        total = term if total is None else total + term
        start += rows
    return total


def on_device(tmatrix, translation, incident, farfield, centres):
    pair_index = lax.axis_index("pair")
    column_half = jnp.bitwise_and(jnp.right_shift(pair_index, LEVEL), 1)
    own_centre = lax.dynamic_index_in_dim(centres, pair_index, 0, keepdims=False)
    other_centre = lax.dynamic_index_in_dim(
        centres, jnp.bitwise_xor(pair_index, 2**LEVEL), 0, keepdims=False
    )
    own_matrix = tmatrix[0]
    own_coupling = translation[0]
    own_incident = incident[0]
    full_width = own_incident.shape[1] // 2
    half_width = full_width // 2
    coeffs = col_sum(product(own_matrix, own_incident)).astype(jnp.bfloat16)
    for _ in range(ITERS):
        half_rows = coeffs.shape[0] // 2
        first_part = partner(coeffs[:half_rows], "pair", LEVEL)
        second_part = partner(coeffs[half_rows:], "pair", LEVEL)
        summed = col_sum(split_product(own_coupling, [first_part, second_part]))
        driven = (own_incident.astype(jnp.float32) + summed).astype(jnp.bfloat16)
        coeffs = col_sum(product(own_matrix, driven)).astype(jnp.bfloat16)
    incoming = partner(pick_half(coeffs, 1 - column_half, half_width), "pair", LEVEL)
    own_half = pick_half(coeffs, column_half, half_width)
    total_rows = farfield.shape[1]
    both = jnp.concatenate([own_half, incoming], axis=1)
    both_turned = jnp.concatenate([turned_block(own_half), turned_block(incoming)], axis=1)
    field = jnp.dot(farfield[0], both, preferred_element_type=jnp.float32) + jnp.dot(
        farfield[1], both_turned, preferred_element_type=jnp.float32
    )
    width = own_half.shape[1]
    merged = rotate(field[:, :width], direction_phase(own_centre, total_rows, total_rows)) + rotate(
        field[:, width:], direction_phase(other_centre, total_rows, total_rows)
    )
    amplitude = col_sum(merged)
    return amplitude[None]


def solution(mesh):
    return jax.shard_map(
        on_device,
        mesh=mesh,
        in_specs=(
            P("pair", None, None, "col"),
            P("pair", None, None, "col"),
            P("pair", "col", None),
            P(None, None, "col"),
            P(),
        ),
        out_specs=P("pair", "col", None),
        check_vma=False,
    )
```

```python
import math

import jax
import jax.numpy as jnp
from jax import lax
from jax.sharding import PartitionSpec as P


ITERS = 3
LEVEL = 2


def partner(value, axis, bit):
    mask = 2**bit
    pairs = [(source, source ^ mask) for source in range(lax.axis_size(axis))]
    return lax.ppermute(value, axis, pairs)


def turned_block(vector):
    half_width = vector.shape[1] // 2
    return jnp.concatenate([-vector[:, half_width:], vector[:, :half_width]], axis=1)


def rotate(field, phase):
    half_width = field.shape[1] // 2
    cosine = jnp.cos(phase)[:, None]
    sine = jnp.sin(phase)[:, None]
    real_part = field[:, :half_width]
    imag_part = field[:, half_width:]
    return jnp.concatenate(
        [cosine * real_part + sine * imag_part, cosine * imag_part - sine * real_part], axis=1
    )


def direction_phase(centre, count, total_rows):
    steps_int = jnp.arange(count, dtype=jnp.int32)
    polar = math.pi / total_rows * (steps_int.astype(jnp.float32) + 0.5)
    azimuth = 2.0 * math.pi / 97.0 * (steps_int * 40 % 97).astype(jnp.float32)
    spot = centre.astype(jnp.float32)
    return 0.7 * (
        jnp.sin(polar) * jnp.cos(azimuth) * spot[0]
        + jnp.sin(polar) * jnp.sin(azimuth) * spot[1]
        + jnp.cos(polar) * spot[2]
    )


def pick_half(vector, column_half, half_width):
    full_width = vector.shape[1] // 2
    real_part = lax.dynamic_slice_in_dim(vector, column_half * half_width, half_width, 1)
    imag_part = lax.dynamic_slice_in_dim(
        vector, full_width + column_half * half_width, half_width, 1
    )
    return jnp.concatenate([real_part, imag_part], axis=1)


def col_sum(partial):
    count = lax.axis_size("col")
    rows, width = partial.shape
    blocks = partial.astype(jnp.bfloat16).reshape(count, rows // count, width)
    received = lax.all_to_all(blocks, "col", 0, 0)
    return jnp.sum(received.astype(jnp.float32), axis=0)


def product(matrix, vector):
    stacked = jnp.stack([vector, turned_block(vector)])
    return jnp.einsum("prc,pck->rk", matrix, stacked, preferred_element_type=jnp.float32)


def split_product(matrix, parts):
    total = None
    start = 0
    for index, piece in enumerate(parts):
        rows = piece.shape[0]
        term = product(matrix[:, :, start : start + rows], piece)
        if index + 1 < len(parts):
            term = lax.optimization_barrier(term)
        total = term if total is None else total + term
        start += rows
    return total


def on_device(tmatrix, translation, incident, farfield, centres):
    pair_index = lax.axis_index("pair")
    column_half = jnp.bitwise_and(jnp.right_shift(pair_index, LEVEL), 1)
    own_centre = lax.dynamic_index_in_dim(centres, pair_index, 0, keepdims=False)
    other_centre = lax.dynamic_index_in_dim(
        centres, jnp.bitwise_xor(pair_index, 2**LEVEL), 0, keepdims=False
    )
    own_matrix = tmatrix[0]
    own_coupling = translation[0]
    own_incident = incident[0]
    full_width = own_incident.shape[1] // 2
    half_width = full_width // 2
    coeffs = col_sum(product(own_matrix, own_incident)).astype(jnp.bfloat16)
    for _ in range(ITERS):
        half_rows = coeffs.shape[0] // 4
        first_part = partner(coeffs[:half_rows], "pair", LEVEL)
        second_part = partner(coeffs[half_rows:], "pair", LEVEL)
        summed = col_sum(split_product(own_coupling, [first_part, second_part]))
        driven = (own_incident.astype(jnp.float32) + summed).astype(jnp.bfloat16)
        coeffs = col_sum(product(own_matrix, driven)).astype(jnp.bfloat16)
    incoming = partner(pick_half(coeffs, 1 - column_half, half_width), "pair", LEVEL)
    own_half = pick_half(coeffs, column_half, half_width)
    total_rows = farfield.shape[1]
    own_field = product(farfield, own_half)
    other_field = product(farfield, incoming)
    merged = rotate(own_field, direction_phase(own_centre, total_rows, total_rows)) + rotate(
        other_field, direction_phase(other_centre, total_rows, total_rows)
    )
    amplitude = col_sum(merged)
    return amplitude[None]


def solution(mesh):
    return jax.shard_map(
        on_device,
        mesh=mesh,
        in_specs=(
            P("pair", None, None, "col"),
            P("pair", None, None, "col"),
            P("pair", "col", None),
            P(None, None, "col"),
            P(),
        ),
        out_specs=P("pair", "col", None),
        check_vma=False,
    )
```

```python
import math

import jax
import jax.numpy as jnp
from jax import lax
from jax.sharding import PartitionSpec as P


ITERS = 3
LEVEL = 2


def partner(value, axis, bit):
    mask = 2**bit
    pairs = [(source, source ^ mask) for source in range(lax.axis_size(axis))]
    return lax.ppermute(value, axis, pairs)


def turned_block(vector):
    half_width = vector.shape[1] // 2
    return jnp.concatenate([-vector[:, half_width:], vector[:, :half_width]], axis=1)


def rotate(field, phase):
    half_width = field.shape[1] // 2
    cosine = jnp.cos(phase)[:, None]
    sine = jnp.sin(phase)[:, None]
    real_part = field[:, :half_width]
    imag_part = field[:, half_width:]
    return jnp.concatenate(
        [cosine * real_part + sine * imag_part, cosine * imag_part - sine * real_part], axis=1
    )


def direction_phase(centre, count, total_rows):
    steps_int = jnp.arange(count, dtype=jnp.int32)
    polar = math.pi / total_rows * (steps_int.astype(jnp.float32) + 0.5)
    azimuth = 2.0 * math.pi / 97.0 * (steps_int * 40 % 97).astype(jnp.float32)
    spot = centre.astype(jnp.float32)
    return 0.7 * (
        jnp.sin(polar) * jnp.cos(azimuth) * spot[0]
        + jnp.sin(polar) * jnp.sin(azimuth) * spot[1]
        + jnp.cos(polar) * spot[2]
    )


def pick_half(vector, column_half, half_width):
    full_width = vector.shape[1] // 2
    real_part = lax.dynamic_slice_in_dim(vector, column_half * half_width, half_width, 1)
    imag_part = lax.dynamic_slice_in_dim(
        vector, full_width + column_half * half_width, half_width, 1
    )
    return jnp.concatenate([real_part, imag_part], axis=1)


def col_sum(partial):
    count = lax.axis_size("col")
    rows, width = partial.shape
    blocks = partial.astype(jnp.bfloat16).reshape(count, rows // count, width)
    received = lax.all_to_all(blocks, "col", 0, 0)
    return jnp.sum(received.astype(jnp.float32), axis=0)


def product(matrix, vector):
    stacked = jnp.stack([vector, turned_block(vector)])
    return jnp.einsum("prc,pck->rk", matrix, stacked, preferred_element_type=jnp.float32)


def split_product(matrix, parts):
    total = None
    for start, piece in parts:
        rows = piece.shape[0]
        term = product(matrix[:, :, start : start + rows], piece)
        if total is None:
            total = lax.optimization_barrier(term)
        else:
            total = term + total
    return total


def on_device(tmatrix, translation, incident, farfield, centres):
    pair_index = lax.axis_index("pair")
    column_half = jnp.bitwise_and(jnp.right_shift(pair_index, LEVEL), 1)
    own_centre = lax.dynamic_index_in_dim(centres, pair_index, 0, keepdims=False)
    other_centre = lax.dynamic_index_in_dim(
        centres, jnp.bitwise_xor(pair_index, 2**LEVEL), 0, keepdims=False
    )
    own_matrix = tmatrix[0]
    own_coupling = translation[0]
    own_incident = incident[0]
    full_width = own_incident.shape[1] // 2
    half_width = full_width // 2
    coeffs = col_sum(product(own_matrix, own_incident)).astype(jnp.bfloat16)
    for _ in range(ITERS):
        half_rows = coeffs.shape[0] // 2
        first_part = partner(coeffs[:half_rows], "pair", LEVEL)
        second_part = partner(coeffs[half_rows:], "pair", LEVEL)
        summed = col_sum(split_product(own_coupling, [(0, first_part), (half_rows, second_part)]))
        driven = (own_incident.astype(jnp.float32) + summed).astype(jnp.bfloat16)
        coeffs = col_sum(product(own_matrix, driven)).astype(jnp.bfloat16)
    outgoing = pick_half(coeffs, 1 - column_half, half_width)
    tail_rows = outgoing.shape[0] // 2
    incoming_parts = [
        partner(outgoing[:tail_rows], "pair", LEVEL),
        partner(outgoing[tail_rows:], "pair", LEVEL),
    ]
    own_half = pick_half(coeffs, column_half, half_width)
    total_rows = farfield.shape[1]
    own_field = product(farfield, own_half)
    other_field = split_product(farfield, [(0, incoming_parts[0]), (tail_rows, incoming_parts[1])])
    merged = rotate(own_field, direction_phase(own_centre, total_rows, total_rows)) + rotate(
        other_field, direction_phase(other_centre, total_rows, total_rows)
    )
    amplitude = col_sum(merged)
    return amplitude[None]


def solution(mesh):
    return jax.shard_map(
        on_device,
        mesh=mesh,
        in_specs=(
            P("pair", None, None, "col"),
            P("pair", None, None, "col"),
            P("pair", "col", None),
            P(None, None, "col"),
            P(),
        ),
        out_specs=P("pair", "col", None),
        check_vma=False,
    )
```

```python
import math

import jax
import jax.numpy as jnp
from jax import lax
from jax.sharding import PartitionSpec as P


ITERS = 3
LEVEL = 2


def partner(value, axis, bit):
    mask = 2**bit
    pairs = [(source, source ^ mask) for source in range(lax.axis_size(axis))]
    return lax.ppermute(value, axis, pairs)


def turned_block(vector):
    half_width = vector.shape[1] // 2
    return jnp.concatenate([-vector[:, half_width:], vector[:, :half_width]], axis=1)


def rotate(field, phase):
    half_width = field.shape[1] // 2
    cosine = jnp.cos(phase)[:, None]
    sine = jnp.sin(phase)[:, None]
    real_part = field[:, :half_width]
    imag_part = field[:, half_width:]
    return jnp.concatenate(
        [cosine * real_part + sine * imag_part, cosine * imag_part - sine * real_part], axis=1
    )


def direction_phase(centre, count, total_rows):
    steps_int = jnp.arange(count, dtype=jnp.int32)
    polar = math.pi / total_rows * (steps_int.astype(jnp.float32) + 0.5)
    azimuth = 2.0 * math.pi / 97.0 * (steps_int * 40 % 97).astype(jnp.float32)
    spot = centre.astype(jnp.float32)
    return 0.7 * (
        jnp.sin(polar) * jnp.cos(azimuth) * spot[0]
        + jnp.sin(polar) * jnp.sin(azimuth) * spot[1]
        + jnp.cos(polar) * spot[2]
    )


def pick_half(vector, column_half, half_width):
    full_width = vector.shape[1] // 2
    real_part = lax.dynamic_slice_in_dim(vector, column_half * half_width, half_width, 1)
    imag_part = lax.dynamic_slice_in_dim(
        vector, full_width + column_half * half_width, half_width, 1
    )
    return jnp.concatenate([real_part, imag_part], axis=1)


def col_sum(partial):
    count = lax.axis_size("col")
    rows, width = partial.shape
    blocks = partial.astype(jnp.bfloat16).reshape(count, rows // count, width)
    received = lax.all_to_all(blocks, "col", 0, 0)
    return jnp.sum(received.astype(jnp.float32), axis=0)


def product(matrix, vector):
    stacked = jnp.stack([vector, turned_block(vector)])
    return jnp.einsum("prc,pck->rk", matrix, stacked, preferred_element_type=jnp.float32)


def split_product(matrix, parts):
    total = None
    for start, piece in parts:
        rows = piece.shape[0]
        term = product(matrix[:, :, start : start + rows], piece)
        if total is None:
            total = lax.optimization_barrier(term)
        else:
            total = term + total
    return total


def on_device(tmatrix, translation, incident, farfield, centres):
    pair_index = lax.axis_index("pair")
    column_half = jnp.bitwise_and(jnp.right_shift(pair_index, LEVEL), 1)
    own_centre = lax.dynamic_index_in_dim(centres, pair_index, 0, keepdims=False)
    other_centre = lax.dynamic_index_in_dim(
        centres, jnp.bitwise_xor(pair_index, 2**LEVEL), 0, keepdims=False
    )
    own_matrix = tmatrix[0]
    own_coupling = translation[0]
    own_incident = incident[0]
    full_width = own_incident.shape[1] // 2
    half_width = full_width // 2
    coeffs = col_sum(product(own_matrix, own_incident)).astype(jnp.bfloat16)
    for _ in range(ITERS):
        half_rows = coeffs.shape[0] // 4
        first_part = partner(coeffs[:half_rows], "pair", LEVEL)
        second_part = partner(coeffs[half_rows:], "pair", LEVEL)
        summed = col_sum(split_product(own_coupling, [(0, first_part), (half_rows, second_part)]))
        driven = (own_incident.astype(jnp.float32) + summed).astype(jnp.bfloat16)
        coeffs = col_sum(product(own_matrix, driven)).astype(jnp.bfloat16)
    incoming = partner(pick_half(coeffs, 1 - column_half, half_width), "pair", LEVEL)
    own_half = pick_half(coeffs, column_half, half_width)
    total_rows = farfield.shape[1]
    own_field = product(farfield, own_half)
    other_field = product(farfield, incoming)
    merged = rotate(own_field, direction_phase(own_centre, total_rows, total_rows)) + rotate(
        other_field, direction_phase(other_centre, total_rows, total_rows)
    )
    amplitude = col_sum(merged)
    return amplitude[None]


def solution(mesh):
    return jax.shard_map(
        on_device,
        mesh=mesh,
        in_specs=(
            P("pair", None, None, "col"),
            P("pair", None, None, "col"),
            P("pair", "col", None),
            P(None, None, "col"),
            P(),
        ),
        out_specs=P("pair", "col", None),
        check_vma=False,
    )
```
